768 devices in a mesh: slab: 8 (over y), kmom: 16 (over z_lo, x), energy: 6 (over z_hi, core).
Axes of the slice: x: 4, y: 8, z: 12 (z_hi: 3, z_lo: 4; z = z_hi * 4 + z_lo), core: 2. Of those that a mesh axis runs over, the one named last changes fastest.
Arguments:
- free_green: float32 [8, 6, 16, 2, 256, 256], P('slab', 'energy', 'kmom'), as said below
- coupling: float32 [8, 256, 256], P('slab'), may hold values from -0.375 to 0.375
- coupling_tiles: int32 [8, 8, 3], P('slab'), may hold values from 0 to 7, as said below
- occupation: float32 [6], P('energy'), may hold values from 0.05 to 1
- phonon_weight: float32 [2, 16, 16], replicated, may hold values from 0.2 to 1
- phonon_mode: int32 [2], replicated, may hold values from 0 to 1, each once
Outputs:
- green: float32 [8, 6, 16, 2, 256, 256], P('slab', 'energy', 'kmom')
- self_energy: bfloat16 [8, 6, 16, 2, 256, 256], P('slab', 'energy', 'kmom')
The draws below stay inside these ranges and needn't reach their ends.
Inputs may be any that keep to these rules, and one draw needn't show every extreme that they name: `coupling_tiles`: the 3 column tiles of one row tile are distinct. `phonon_mode`: each value once. `free_green`: the imaginary part of every diagonal entry is negative.
All inputs are finite; a program needn't handle non-finite values.
Results may differ from the reference program's by a relative error of at most 0.0034.
Values may be sent and summed in bfloat16 or wider, within the bound.
No kernel may reach another device: no remote copies, remote signals or barrier semaphores. Data moves between devices by JAX's collectives and lax.ppermute only.
A program may use at most 32 MiB of HBM per device.

```python
import math
import jax
import jax.numpy as jnp
from jax import lax

NB = 256
NTILE = 8
NNZ = 3
BRANCHES = 2
NSLAB = 8
ENERGIES = 6
MOMENTA = 16


def draw_free_green(key, part):
    key_sym, key_anti, key_common, key_diag = jax.random.split(key, 4)
    shape = (NSLAB, ENERGIES, MOMENTA, 2, NB, NB)
    anti_shape = (NSLAB, ENERGIES, MOMENTA, NB, NB)
    common_shape = (NSLAB, 1, 1, NB, NB)
    sym_noise = jax.random.normal(key_sym, shape, jnp.float32)
    anti_noise = jax.random.normal(key_anti, anti_shape, jnp.float32)
    common_noise = jax.random.normal(key_common, common_shape, jnp.float32)
    scale = 1.0 / jnp.sqrt(2.0 * NB)
    symmetric = 0.3 * (sym_noise + jnp.swapaxes(sym_noise, -1, -2)) * scale
    anti_own = anti_noise - jnp.swapaxes(anti_noise, -1, -2)
    anti_common = common_noise - jnp.swapaxes(common_noise, -1, -2)
    anti_real = 0.6 * (anti_own + anti_common) * scale
    antisymmetric = jnp.stack([anti_real, jnp.zeros_like(anti_real)], axis=3)
    diag_draw = jax.random.uniform(key_diag, (NSLAB, ENERGIES, MOMENTA, 2, NB), jnp.float32)
    diag_real = 2.0 * diag_draw[:, :, :, 0, :] - 1.0
    diag_imag = -(0.3 + 1.2 * diag_draw[:, :, :, 1, :])
    diagonal = jnp.stack([diag_real, diag_imag], axis=3)
    identity = jnp.eye(NB, dtype=jnp.float32)
    return symmetric + antisymmetric + diagonal[..., None] * identity


def draw_coupling_tiles(key, part):
    keys = jax.random.split(key, NSLAB * NTILE)
    picked = jax.vmap(lambda single: jax.random.permutation(single, NTILE)[:NNZ])(keys)
    return picked.reshape(NSLAB, NTILE, NNZ).astype(jnp.int32)


def steps_of(own_key, shape, pieces, low, top_value):
    gain, own = 1.0, jax.random.fold_in(own_key, 6)
    for dim, blocks in pieces:
        steps = jnp.exp(jax.random.uniform(jax.random.fold_in(own, dim), (blocks,), jnp.float32, low / len(pieces), top_value / len(pieces)))
        gain = gain * jnp.repeat(steps, shape[dim] // blocks).reshape([-1 if axis == dim else 1 for axis in range(len(shape))])
    return gain


def centred(rng, shape, spread, limit, pieces=(), kind=jnp.bfloat16):
    array = jax.random.normal(rng, shape, jnp.float32) * spread
    if len(pieces) > 0:
        array = steps_of(rng, shape, pieces, -0.22, 0.18) * array
    return jnp.clip(array, min=-limit, max=limit).astype(kind)


def setup_inputs(seed: int = 0) -> dict:
    key_of = jax.random.split(jax.random.key(seed), 7)
    return {
        "free_green": draw_free_green(jax.random.fold_in(key_of[6], 71), 0),
        "coupling": centred(key_of[1], (NSLAB, NB, NB), NB ** -0.5, 0.375, ((0, 8),), jnp.float32),
        "coupling_tiles": draw_coupling_tiles(jax.random.fold_in(key_of[6], 71), 0),
        "occupation": jnp.clip(0.05 + 0.95 * jax.random.uniform(key_of[3], (ENERGIES,), jnp.float32) ** steps_of(key_of[3], (ENERGIES,), ((0, 6),), -0.2, 0.2), 0.05, 1.0),
        "phonon_weight": jnp.clip(jnp.exp(jax.random.uniform(key_of[4], (BRANCHES, MOMENTA, MOMENTA), jnp.float32, math.log(0.2), math.log(1.0))), 0.2, 1.0),
        "phonon_mode": jax.random.permutation(key_of[5], BRANCHES).astype(jnp.int32),
    }


def complex_product(left_factor, right_factor):
    left_real = left_factor[..., 0, :, :]
    left_imag = left_factor[..., 1, :, :]
    right_real = right_factor[..., 0, :, :]
    right_imag = right_factor[..., 1, :, :]
    highest = lax.Precision.HIGHEST
    real_part = jnp.matmul(left_real, right_real, precision=highest) - jnp.matmul(left_imag, right_imag, precision=highest)
    imag_part = jnp.matmul(left_real, right_imag, precision=highest) + jnp.matmul(left_imag, right_real, precision=highest)
    return jnp.stack([real_part, imag_part], axis=-3)


def sandwich(pair_map, inner):
    return complex_product(complex_product(pair_map, inner), jnp.swapaxes(pair_map, -1, -2))


def self_energy_of(green_blocks, occupation, phonon_weight, shifts):
    filling = occupation[:, None, None, None]
    real_part = -filling * (green_blocks[:, :, 0] - jnp.swapaxes(green_blocks[:, :, 0], -1, -2))
    imag_part = -filling * (green_blocks[:, :, 1] + jnp.swapaxes(green_blocks[:, :, 1], -1, -2))
    lesser = jnp.stack([real_part, imag_part], axis=2).astype(jnp.bfloat16)
    lesser = lax.optimization_barrier(lesser).astype(jnp.float32)
    padded = jnp.pad(lesser, ((1, 1), (0, 0), (0, 0), (0, 0), (0, 0)))
    summed = jnp.zeros(lesser.shape, jnp.float32)
    for branch in range(BRANCHES):
        shift_now = shifts[branch]
        upper_slice = lax.dynamic_slice_in_dim(padded, 1 + shift_now, ENERGIES, 0)
        lower_slice = lax.dynamic_slice_in_dim(padded, 1 - shift_now, ENERGIES, 0)
        summed = summed + jnp.einsum('kq,eqcij->ekcij', phonon_weight[branch], upper_slice + lower_slice, precision=lax.Precision.HIGHEST)
    return summed.astype(jnp.bfloat16)


def reference(free_green, coupling, coupling_tiles, occupation, phonon_weight, phonon_mode):
    tile_size = NB // NTILE
    column_tile = jnp.arange(NB, dtype=jnp.int32) // tile_size
    tile_hit = jnp.any(coupling_tiles[..., None] == column_tile, axis=-2).astype(jnp.float32)
    tile_mask = jnp.repeat(tile_hit, tile_size, axis=1)
    coupled = coupling * tile_mask
    shifts = phonon_mode.astype(jnp.int32)
    beyond = jnp.zeros(free_green.shape[1:], jnp.float32)
    greens = []
    selfs = []
    for index in range(NSLAB - 1, -1, -1):
        pair_map = jnp.einsum('ekcij,jl->ekcil', free_green[index], coupled[index], precision=lax.Precision.HIGHEST)
        beyond = free_green[index] + sandwich(pair_map, beyond)
        greens.append(beyond)
        selfs.append(self_energy_of(beyond, occupation, phonon_weight, shifts))
    return jnp.stack(greens[::-1]), jnp.stack(selfs[::-1])
```

```python
import jax
import jax.numpy as jnp
from jax import lax
from jax.sharding import PartitionSpec as P


def passed_along(shard, axis, by):
    length = lax.axis_size(axis)
    pairs = [(i, i + by) for i in range(length) if 0 <= i + by < length]
    return lax.ppermute(shard, axis, pairs)


def complex_product(left_factor, right_factor):
    left_real = left_factor[..., 0, :, :]
    left_imag = left_factor[..., 1, :, :]
    right_real = right_factor[..., 0, :, :]
    right_imag = right_factor[..., 1, :, :]
    highest = lax.Precision.HIGHEST
    real_part = jnp.matmul(left_real, right_real, precision=highest) - jnp.matmul(
        left_imag, right_imag, precision=highest
    )
    imag_part = jnp.matmul(left_real, right_imag, precision=highest) + jnp.matmul(
        left_imag, right_real, precision=highest
    )
    return jnp.stack([real_part, imag_part], axis=-3)


def sandwich(pair_map, inner):
    return complex_product(complex_product(pair_map, inner), jnp.swapaxes(pair_map, -1, -2))


def self_energy_of(green, occupation, phonon_weight, phonon_mode):
    filling = occupation[0]
    real_part = -filling * (green[0] - green[0].T)
    imag_part = -filling * (green[1] + green[1].T)
    lesser = jnp.stack([real_part, imag_part], axis=0).astype(jnp.bfloat16)
    width = lesser.shape[-1]
    moms = lax.axis_size("kmom")
    rows = width // moms
    chunks = lesser.reshape(2, moms, rows, width).transpose(1, 0, 2, 3)
    held = lax.all_to_all(chunks, "kmom", 0, 0)
    below = passed_along(held, "energy", 1)
    above = passed_along(held, "energy", -1)
    flat = held.reshape(moms, -1).astype(jnp.float32)
    near = below.reshape(moms, -1).astype(jnp.float32) + above.reshape(moms, -1).astype(jnp.float32)
    still = phonon_mode[0] == 0
    weight_still = jnp.where(still, phonon_weight[0], phonon_weight[1])
    weight_moved = jnp.where(still, phonon_weight[1], phonon_weight[0])
    summed = jnp.matmul(
        weight_still, flat + flat, precision=lax.Precision.HIGHEST
    ) + jnp.matmul(weight_moved, near, precision=lax.Precision.HIGHEST)
    out = summed.astype(jnp.bfloat16).reshape(moms, 2, rows, width)
    back = lax.all_to_all(out, "kmom", 0, 0)
    return back.transpose(1, 0, 2, 3).reshape(2, width, width)


def on_device(free_green, coupling, coupling_tiles, occupation, phonon_weight, phonon_mode):
    slab_count = free_green.shape[0]
    block_width = coupling.shape[-1]
    tile_count = coupling_tiles.shape[1]
    tile_size = block_width // tile_count
    column_tile = jnp.arange(block_width, dtype=jnp.int32) // tile_size
    tile_hit = jnp.any(coupling_tiles[..., None] == column_tile, axis=-2).astype(jnp.float32)
    tile_mask = jnp.broadcast_to(
        tile_hit[:, :, None, :], (slab_count, tile_count, tile_size, block_width)
    ).reshape(slab_count, block_width, block_width)
    coupled = coupling * tile_mask
    pair_map = jnp.einsum(
        "ekcij,jl->ekcil", free_green[0], coupled[0], precision=lax.Precision.HIGHEST
    )

    def sweep(beyond):
        return free_green[0] + sandwich(pair_map, beyond)

    zero_block = jnp.zeros(free_green.shape[1:], jnp.float32)

    def advance(turn_index, beyond):
        return passed_along(sweep(beyond), "slab", -1)

    beyond = lax.fori_loop(0, lax.axis_size("slab") - 1, advance, zero_block)
    green = sweep(beyond)
    self_energy = self_energy_of(green[0, 0], occupation, phonon_weight, phonon_mode)
    return green[None], self_energy.reshape(green.shape)[None]


def solution(mesh):
    in_specs = (
        P("slab", "energy", "kmom", None, None, None),
        P("slab", None, None),
        P("slab", None, None),
        P("energy"),
        P(),
        P(),
    )
    out_specs = (
        P("slab", "energy", "kmom", None, None, None),
        P("slab", "energy", "kmom", None, None, None),
    )
    return jax.shard_map(
        on_device, mesh=mesh, in_specs=in_specs, out_specs=out_specs, check_vma=False
    )
```

```python
import jax
import jax.numpy as jnp
from jax import lax
from jax.sharding import PartitionSpec as P


def passed_along(shard, axis, by):
    length = lax.axis_size(axis)
    pairs = [(i, i + by) for i in range(length) if 0 <= i + by < length]
    return lax.ppermute(shard, axis, pairs)


def complex_product(left_factor, right_factor):
    left_real = left_factor[..., 0, :, :]
    left_imag = left_factor[..., 1, :, :]
    right_real = right_factor[..., 0, :, :]
    right_imag = right_factor[..., 1, :, :]
    high = lax.Precision.HIGH
    real_part = jnp.matmul(left_real, right_real, precision=high) - jnp.matmul(
        left_imag, right_imag, precision=high
    )
    imag_part = jnp.matmul(left_real, right_imag, precision=high) + jnp.matmul(
        left_imag, right_real, precision=high
    )
    return jnp.stack([real_part, imag_part], axis=-3)


def sandwich(pair_map, inner):
    return complex_product(complex_product(pair_map, inner), jnp.swapaxes(pair_map, -1, -2))


def self_energy_of(green, occupation, phonon_weight, phonon_mode):
    filling = occupation[0]
    real_part = -filling * (green[0] - green[0].T)
    imag_part = -filling * (green[1] + green[1].T)
    lesser = jnp.stack([real_part, imag_part], axis=0).astype(jnp.bfloat16)
    width = lesser.shape[-1]
    moms = lax.axis_size("kmom")
    rows = width // moms
    chunks = lesser.reshape(2, moms, rows, width).transpose(1, 0, 2, 3)
    held = lax.all_to_all(chunks, "kmom", 0, 0)
    below = passed_along(held, "energy", 1)
    above = passed_along(held, "energy", -1)
    flat = held.reshape(moms, -1).astype(jnp.float32)
    near = below.reshape(moms, -1).astype(jnp.float32) + above.reshape(moms, -1).astype(jnp.float32)
    still = phonon_mode[0] == 0
    weight_still = jnp.where(still, phonon_weight[0], phonon_weight[1])
    weight_moved = jnp.where(still, phonon_weight[1], phonon_weight[0])
    summed = jnp.matmul(
        weight_still, flat + flat, precision=lax.Precision.HIGHEST
    ) + jnp.matmul(weight_moved, near, precision=lax.Precision.HIGHEST)
    out = summed.astype(jnp.bfloat16).reshape(moms, 2, rows, width)
    back = lax.all_to_all(out, "kmom", 0, 0)
    return back.transpose(1, 0, 2, 3).reshape(2, width, width)


def on_device(free_green, coupling, coupling_tiles, occupation, phonon_weight, phonon_mode):
    slab_count = free_green.shape[0]
    block_width = coupling.shape[-1]
    tile_count = coupling_tiles.shape[1]
    tile_size = block_width // tile_count
    column_tile = jnp.arange(block_width, dtype=jnp.int32) // tile_size
    tile_hit = jnp.any(coupling_tiles[..., None] == column_tile, axis=-2).astype(jnp.float32)
    tile_mask = jnp.broadcast_to(
        tile_hit[:, :, None, :], (slab_count, tile_count, tile_size, block_width)
    ).reshape(slab_count, block_width, block_width)
    coupled = coupling * tile_mask
    pair_map = jnp.einsum(
        "ekcij,jl->ekcil", free_green[0], coupled[0], precision=lax.Precision.HIGHEST
    )

    def sweep(beyond):
        return free_green[0] + sandwich(pair_map, beyond)

    def advance(turn_index, beyond):
        return passed_along(sweep(beyond), "slab", -1)

    first = passed_along(free_green[0], "slab", -1)
    beyond = lax.fori_loop(0, lax.axis_size("slab") - 2, advance, first)
    green = sweep(beyond)
    self_energy = self_energy_of(green[0, 0], occupation, phonon_weight, phonon_mode)
    return green[None], self_energy.reshape(green.shape)[None]


def solution(mesh):
    in_specs = (
        P("slab", "energy", "kmom", None, None, None),
        P("slab", None, None),
        P("slab", None, None),
        P("energy"),
        P(),
        P(),
    )
    out_specs = (
        P("slab", "energy", "kmom", None, None, None),
        P("slab", "energy", "kmom", None, None, None),
    )
    return jax.shard_map(
        on_device, mesh=mesh, in_specs=in_specs, out_specs=out_specs, check_vma=False
    )
```

```python
import jax
import jax.numpy as jnp
from jax import lax
from jax.sharding import PartitionSpec as P


def passed_along(shard, axis, by):
    length = lax.axis_size(axis)
    pairs = [(i, i + by) for i in range(length) if 0 <= i + by < length]
    return lax.ppermute(shard, axis, pairs)


def complex_product(left_factor, right_factor):
    left_real = left_factor[..., 0, :, :]
    left_imag = left_factor[..., 1, :, :]
    right_real = right_factor[..., 0, :, :]
    right_imag = right_factor[..., 1, :, :]
    high = lax.Precision.HIGH
    real_part = jnp.matmul(left_real, right_real, precision=high) - jnp.matmul(
        left_imag, right_imag, precision=high
    )
    imag_part = jnp.matmul(left_real, right_imag, precision=high) + jnp.matmul(
        left_imag, right_real, precision=high
    )
    return jnp.stack([real_part, imag_part], axis=-3)


def sandwich(pair_map, inner):
    return complex_product(complex_product(pair_map, inner), jnp.swapaxes(pair_map, -1, -2))


def self_energy_of(green, occupation, phonon_weight, phonon_mode):
    filling = occupation[0]
    real_part = -filling * (green[0] - green[0].T)
    imag_part = -filling * (green[1] + green[1].T)
    lesser = jnp.stack([real_part, imag_part], axis=0).astype(jnp.bfloat16)
    width = lesser.shape[-1]
    moms = lax.axis_size("kmom")
    rows = width // moms
    chunks = lesser.reshape(2, moms, rows, width).transpose(1, 0, 2, 3)
    held = lax.all_to_all(chunks, "kmom", 0, 0)
    below = passed_along(held, "energy", 1)
    above = passed_along(held, "energy", -1)
    flat = held.reshape(moms, -1).astype(jnp.float32)
    near = below.reshape(moms, -1).astype(jnp.float32) + above.reshape(moms, -1).astype(jnp.float32)
    still = phonon_mode[0] == 0
    weight_still = jnp.where(still, phonon_weight[0], phonon_weight[1])
    weight_moved = jnp.where(still, phonon_weight[1], phonon_weight[0])
    summed = jnp.matmul(
        weight_still, flat + flat, precision=lax.Precision.HIGHEST
    ) + jnp.matmul(weight_moved, near, precision=lax.Precision.HIGHEST)
    out = summed.astype(jnp.bfloat16).reshape(moms, 2, rows, width)
    back = lax.all_to_all(out, "kmom", 0, 0)
    return back.transpose(1, 0, 2, 3).reshape(2, width, width)


def on_device(free_green, coupling, coupling_tiles, occupation, phonon_weight, phonon_mode):
    slab_count = free_green.shape[0]
    block_width = coupling.shape[-1]
    tile_count = coupling_tiles.shape[1]
    tile_size = block_width // tile_count
    column_tile = jnp.arange(block_width, dtype=jnp.int32) // tile_size
    tile_hit = jnp.any(coupling_tiles[..., None] == column_tile, axis=-2).astype(jnp.float32)
    tile_mask = jnp.broadcast_to(
        tile_hit[:, :, None, :], (slab_count, tile_count, tile_size, block_width)
    ).reshape(slab_count, block_width, block_width)
    coupled = coupling * tile_mask
    pair_map = jnp.einsum(
        "ekcij,jl->ekcil", free_green[0], coupled[0], precision=lax.Precision.HIGHEST
    )[0, 0]
    map_real, map_imag = pair_map[0], pair_map[1]
    left_block = jnp.concatenate(
        [
            jnp.concatenate([map_real, -map_imag], axis=1),
            jnp.concatenate([map_imag, map_real], axis=1),
        ],
        axis=0,
    )
    right_block = jnp.concatenate([map_real.T, map_imag.T], axis=1)
    width = block_width
    high = lax.Precision.HIGH

    def sweep(beyond):
        inner = beyond.reshape(2 * width, width)
        mixed = jnp.matmul(left_block, inner, precision=high)
        outer = jnp.matmul(mixed, right_block, precision=high)
        real_part = outer[:width, :width] - outer[width:, width:]
        imag_part = outer[:width, width:] + outer[width:, :width]
        return free_green[0] + jnp.stack([real_part, imag_part], axis=0)[None, None]

    def advance(turn_index, beyond):
        return passed_along(sweep(beyond), "slab", -1)

    first = passed_along(free_green[0], "slab", -1)
    beyond = lax.fori_loop(0, lax.axis_size("slab") - 2, advance, first)
    green = sweep(beyond)
    self_energy = self_energy_of(green[0, 0], occupation, phonon_weight, phonon_mode)
    return green[None], self_energy.reshape(green.shape)[None]


def solution(mesh):
    in_specs = (
        P("slab", "energy", "kmom", None, None, None),
        P("slab", None, None),
        P("slab", None, None),
        P("energy"),
        P(),
        P(),
    )
    out_specs = (
        P("slab", "energy", "kmom", None, None, None),
        P("slab", "energy", "kmom", None, None, None),
    )
    return jax.shard_map(
        on_device, mesh=mesh, in_specs=in_specs, out_specs=out_specs, check_vma=False
    )
```

```python
import jax
import jax.numpy as jnp
from jax import lax
from jax.sharding import PartitionSpec as P


def passed_along(shard, axis, by):
    length = lax.axis_size(axis)
    pairs = [(i, i + by) for i in range(length) if 0 <= i + by < length]
    return lax.ppermute(shard, axis, pairs)


def complex_product(left_factor, right_factor):
    left_real = left_factor[..., 0, :, :]
    left_imag = left_factor[..., 1, :, :]
    right_real = right_factor[..., 0, :, :]
    right_imag = right_factor[..., 1, :, :]
    high = lax.Precision.HIGH
    real_part = jnp.matmul(left_real, right_real, precision=high) - jnp.matmul(
        left_imag, right_imag, precision=high
    )
    imag_part = jnp.matmul(left_real, right_imag, precision=high) + jnp.matmul(
        left_imag, right_real, precision=high
    )
    return jnp.stack([real_part, imag_part], axis=-3)


def sandwich(pair_map, inner):
    return complex_product(complex_product(pair_map, inner), jnp.swapaxes(pair_map, -1, -2))


def self_energy_of(green, occupation, phonon_weight, phonon_mode):
    filling = occupation[0]
    real_part = -filling * (green[0] - green[0].T)
    imag_part = -filling * (green[1] + green[1].T)
    lesser = jnp.stack([real_part, imag_part], axis=0).astype(jnp.bfloat16)
    width = lesser.shape[-1]
    moms = lax.axis_size("kmom")
    rows = width // moms
    chunks = lesser.reshape(2, moms, rows, width).transpose(1, 0, 2, 3)
    below = passed_along(lesser, "energy", 1)
    above = passed_along(lesser, "energy", -1)
    held = lax.all_to_all(chunks, "kmom", 0, 0)
    sides = jnp.stack([below, above], axis=0).reshape(2, 2, moms, rows, width).transpose(2, 0, 1, 3, 4)
    held_sides = lax.all_to_all(sides, "kmom", 0, 0)
    flat = held.reshape(moms, -1).astype(jnp.float32)
    near = held_sides[:, 0].reshape(moms, -1).astype(jnp.float32) + held_sides[:, 1].reshape(
        moms, -1
    ).astype(jnp.float32)
    still = phonon_mode[0] == 0
    weight_still = jnp.where(still, phonon_weight[0], phonon_weight[1])
    weight_moved = jnp.where(still, phonon_weight[1], phonon_weight[0])
    summed = jnp.matmul(
        weight_still, flat + flat, precision=lax.Precision.HIGHEST
    ) + jnp.matmul(weight_moved, near, precision=lax.Precision.HIGHEST)
    out = summed.astype(jnp.bfloat16).reshape(moms, 2, rows, width)
    back = lax.all_to_all(out, "kmom", 0, 0)
    return back.transpose(1, 0, 2, 3).reshape(2, width, width)


def on_device(free_green, coupling, coupling_tiles, occupation, phonon_weight, phonon_mode):
    slab_count = free_green.shape[0]
    block_width = coupling.shape[-1]
    tile_count = coupling_tiles.shape[1]
    tile_size = block_width // tile_count
    column_tile = jnp.arange(block_width, dtype=jnp.int32) // tile_size
    tile_hit = jnp.any(coupling_tiles[..., None] == column_tile, axis=-2).astype(jnp.float32)
    tile_mask = jnp.broadcast_to(
        tile_hit[:, :, None, :], (slab_count, tile_count, tile_size, block_width)
    ).reshape(slab_count, block_width, block_width)
    coupled = coupling * tile_mask
    pair_map = jnp.einsum(
        "ekcij,jl->ekcil", free_green[0], coupled[0], precision=lax.Precision.HIGHEST
    )[0, 0]
    map_real, map_imag = pair_map[0], pair_map[1]
    left_block = jnp.concatenate(
        [
            jnp.concatenate([map_real, -map_imag], axis=1),
            jnp.concatenate([map_imag, map_real], axis=1),
        ],
        axis=0,
    )
    right_block = jnp.concatenate([map_real.T, map_imag.T], axis=1)
    width = block_width
    high = lax.Precision.HIGH

    def sweep(beyond):
        inner = beyond.reshape(2 * width, width)
        mixed = jnp.matmul(left_block, inner, precision=high)
        outer = jnp.matmul(mixed, right_block, precision=high)
        real_part = outer[:width, :width] - outer[width:, width:]
        imag_part = outer[:width, width:] + outer[width:, :width]
        return free_green[0] + jnp.stack([real_part, imag_part], axis=0)[None, None]

    def advance(turn_index, beyond):
        return passed_along(sweep(beyond), "slab", -1)

    first = passed_along(free_green[0], "slab", -1)
    beyond = lax.fori_loop(0, lax.axis_size("slab") - 2, advance, first)
    green = sweep(beyond)
    self_energy = self_energy_of(green[0, 0], occupation, phonon_weight, phonon_mode)
    return green[None], self_energy.reshape(green.shape)[None]


def solution(mesh):
    in_specs = (
        P("slab", "energy", "kmom", None, None, None),
        P("slab", None, None),
        P("slab", None, None),
        P("energy"),
        P(),
        P(),
    )
    out_specs = (
        P("slab", "energy", "kmom", None, None, None),
        P("slab", "energy", "kmom", None, None, None),
    )
    return jax.shard_map(
        on_device, mesh=mesh, in_specs=in_specs, out_specs=out_specs, check_vma=False
    )
```

```python
import jax
import jax.numpy as jnp
from jax import lax
from jax.sharding import PartitionSpec as P


def passed_along(shard, axis, by):
    length = lax.axis_size(axis)
    pairs = [(i, i + by) for i in range(length) if 0 <= i + by < length]
    return lax.ppermute(shard, axis, pairs)


def complex_product(left_factor, right_factor):
    left_real = left_factor[..., 0, :, :]
    left_imag = left_factor[..., 1, :, :]
    right_real = right_factor[..., 0, :, :]
    right_imag = right_factor[..., 1, :, :]
    high = lax.Precision.HIGH
    real_part = jnp.matmul(left_real, right_real, precision=high) - jnp.matmul(
        left_imag, right_imag, precision=high
    )
    imag_part = jnp.matmul(left_real, right_imag, precision=high) + jnp.matmul(
        left_imag, right_real, precision=high
    )
    return jnp.stack([real_part, imag_part], axis=-3)


def sandwich(pair_map, inner):
    return complex_product(complex_product(pair_map, inner), jnp.swapaxes(pair_map, -1, -2))


def self_energy_of(green, occupation, phonon_weight, phonon_mode):
    filling = occupation[0]
    real_part = -filling * (green[0] - green[0].T)
    imag_part = -filling * (green[1] + green[1].T)
    lesser = jnp.stack([real_part, imag_part], axis=0).astype(jnp.bfloat16)
    width = lesser.shape[-1]
    moms = lax.axis_size("kmom")
    rows = width // moms
    chunks = lesser.reshape(2, moms, rows, width).transpose(1, 0, 2, 3)
    held = lax.all_to_all(chunks, "kmom", 0, 0)
    count = lax.axis_size("energy")
    within = [(i, i ^ 1) for i in range(count) if (i ^ 1) < count]
    across = [(i, i + 1 if i % 2 else i - 1) for i in range(count)]
    across = [(i, j) for i, j in across if 0 <= j < count]
    beside = lax.ppermute(held, "energy", within)
    facing = lax.ppermute(held, "energy", across)
    flat = held.reshape(moms, -1).astype(jnp.float32)
    near = beside.reshape(moms, -1).astype(jnp.float32) + facing.reshape(moms, -1).astype(jnp.float32)
    still = phonon_mode[0] == 0
    weight_still = jnp.where(still, phonon_weight[0], phonon_weight[1])
    weight_moved = jnp.where(still, phonon_weight[1], phonon_weight[0])
    summed = jnp.matmul(
        weight_still, flat + flat, precision=lax.Precision.HIGHEST
    ) + jnp.matmul(weight_moved, near, precision=lax.Precision.HIGHEST)
    out = summed.astype(jnp.bfloat16).reshape(moms, 2, rows, width)
    back = lax.all_to_all(out, "kmom", 0, 0)
    return back.transpose(1, 0, 2, 3).reshape(2, width, width)


def on_device(free_green, coupling, coupling_tiles, occupation, phonon_weight, phonon_mode):
    slab_count = free_green.shape[0]
    block_width = coupling.shape[-1]
    tile_count = coupling_tiles.shape[1]
    tile_size = block_width // tile_count
    column_tile = jnp.arange(block_width, dtype=jnp.int32) // tile_size
    tile_hit = jnp.any(coupling_tiles[..., None] == column_tile, axis=-2).astype(jnp.float32)
    tile_mask = jnp.broadcast_to(
        tile_hit[:, :, None, :], (slab_count, tile_count, tile_size, block_width)
    ).reshape(slab_count, block_width, block_width)
    coupled = coupling * tile_mask
    pair_map = jnp.einsum(
        "ekcij,jl->ekcil", free_green[0], coupled[0], precision=lax.Precision.HIGHEST
    )[0, 0]
    map_real, map_imag = pair_map[0], pair_map[1]
    left_block = jnp.concatenate(
        [
            jnp.concatenate([map_real, -map_imag], axis=1),
            jnp.concatenate([map_imag, map_real], axis=1),
        ],
        axis=0,
    )
    right_block = jnp.concatenate([map_real.T, map_imag.T], axis=1)
    left_block, right_block = lax.optimization_barrier((left_block, right_block))
    width = block_width
    high = lax.Precision.HIGH

    def sweep(beyond):
        inner = beyond.reshape(2 * width, width)
        mixed = jnp.matmul(left_block, inner, precision=high)
        outer = jnp.matmul(mixed, right_block, precision=high)
        real_part = outer[:width, :width] - outer[width:, width:]
        imag_part = outer[:width, width:] + outer[width:, :width]
        return free_green[0] + jnp.stack([real_part, imag_part], axis=0)[None, None]

    def advance(turn_index, beyond):
        return passed_along(sweep(beyond), "slab", -1)

    first = passed_along(free_green[0], "slab", -1)
    beyond = lax.fori_loop(0, lax.axis_size("slab") - 2, advance, first)
    green = sweep(beyond)
    self_energy = self_energy_of(green[0, 0], occupation, phonon_weight, phonon_mode)
    return green[None], self_energy.reshape(green.shape)[None]


def solution(mesh):
    in_specs = (
        P("slab", "energy", "kmom", None, None, None),
        P("slab", None, None),
        P("slab", None, None),
        P("energy"),
        P(),
        P(),
    )
    out_specs = (
        P("slab", "energy", "kmom", None, None, None),
        P("slab", "energy", "kmom", None, None, None),
    )
    return jax.shard_map(
        on_device, mesh=mesh, in_specs=in_specs, out_specs=out_specs, check_vma=False
    )
```

```python
import jax
import jax.numpy as jnp
from jax import lax
from jax.sharding import PartitionSpec as P


def passed_along(shard, axis, by):
    length = lax.axis_size(axis)
    pairs = [(i, i + by) for i in range(length) if 0 <= i + by < length]
    return lax.ppermute(shard, axis, pairs)


def complex_product(left_factor, right_factor):
    left_real = left_factor[..., 0, :, :]
    left_imag = left_factor[..., 1, :, :]
    right_real = right_factor[..., 0, :, :]
    right_imag = right_factor[..., 1, :, :]
    high = lax.Precision.HIGH
    real_part = jnp.matmul(left_real, right_real, precision=high) - jnp.matmul(
        left_imag, right_imag, precision=high
    )
    imag_part = jnp.matmul(left_real, right_imag, precision=high) + jnp.matmul(
        left_imag, right_real, precision=high
    )
    return jnp.stack([real_part, imag_part], axis=-3)


def sandwich(pair_map, inner):
    return complex_product(complex_product(pair_map, inner), jnp.swapaxes(pair_map, -1, -2))


def self_energy_of(green, occupation, phonon_weight, phonon_mode):
    filling = occupation[0]
    width = green.shape[-1]
    row = lax.broadcasted_iota(jnp.int32, (width, width), 0)
    col = lax.broadcasted_iota(jnp.int32, (width, width), 1)
    above_diagonal = col > row
    packed = jnp.where(
        above_diagonal,
        -filling * (green[0] - green[0].T),
        -filling * (green[1] + green[1].T),
    ).astype(jnp.bfloat16)
    moms = lax.axis_size("kmom")
    rows = width // moms
    held = lax.all_to_all(packed.reshape(moms, rows, width), "kmom", 0, 0)
    count = lax.axis_size("energy")
    within = [(i, i ^ 1) for i in range(count) if (i ^ 1) < count]
    across = [(i, i + 1 if i % 2 else i - 1) for i in range(count)]
    across = [(i, j) for i, j in across if 0 <= j < count]
    beside = lax.ppermute(held, "energy", within)
    facing = lax.ppermute(held, "energy", across)
    flat = held.reshape(moms, -1).astype(jnp.float32)
    near = beside.reshape(moms, -1).astype(jnp.float32) + facing.reshape(moms, -1).astype(jnp.float32)
    still = phonon_mode[0] == 0
    weight_still = jnp.where(still, phonon_weight[0], phonon_weight[1])
    weight_moved = jnp.where(still, phonon_weight[1], phonon_weight[0])
    summed = jnp.matmul(
        weight_still, flat + flat, precision=lax.Precision.HIGHEST
    ) + jnp.matmul(weight_moved, near, precision=lax.Precision.HIGHEST)
    out = summed.astype(jnp.bfloat16).reshape(moms, rows, width)
    back = lax.all_to_all(out, "kmom", 0, 0).reshape(width, width)
    mirrored = back.T
    real_part = jnp.where(above_diagonal, back, jnp.where(col < row, -mirrored, jnp.zeros_like(back)))
    imag_part = jnp.where(above_diagonal, mirrored, back)
    return jnp.stack([real_part, imag_part], axis=0)


def on_device(free_green, coupling, coupling_tiles, occupation, phonon_weight, phonon_mode):
    slab_count = free_green.shape[0]
    block_width = coupling.shape[-1]
    tile_count = coupling_tiles.shape[1]
    tile_size = block_width // tile_count
    column_tile = jnp.arange(block_width, dtype=jnp.int32) // tile_size
    tile_hit = jnp.any(coupling_tiles[..., None] == column_tile, axis=-2).astype(jnp.float32)
    tile_mask = jnp.broadcast_to(
        tile_hit[:, :, None, :], (slab_count, tile_count, tile_size, block_width)
    ).reshape(slab_count, block_width, block_width)
    coupled = coupling * tile_mask
    pair_map = jnp.einsum(
        "ekcij,jl->ekcil", free_green[0], coupled[0], precision=lax.Precision.HIGHEST
    )[0, 0]
    map_real, map_imag = pair_map[0], pair_map[1]
    left_block = jnp.concatenate(
        [
            jnp.concatenate([map_real, -map_imag], axis=1),
            jnp.concatenate([map_imag, map_real], axis=1),
        ],
        axis=0,
    )
    right_block = jnp.concatenate([map_real.T, map_imag.T], axis=1)
    left_block, right_block = lax.optimization_barrier((left_block, right_block))
    width = block_width
    high = lax.Precision.HIGH

    def sweep(beyond):
        inner = beyond.reshape(2 * width, width)
        mixed = jnp.matmul(left_block, inner, precision=high)
        outer = jnp.matmul(mixed, right_block, precision=high)
        real_part = outer[:width, :width] - outer[width:, width:]
        imag_part = outer[:width, width:] + outer[width:, :width]
        return free_green[0] + jnp.stack([real_part, imag_part], axis=0)[None, None]

    def advance(turn_index, beyond):
        return passed_along(sweep(beyond), "slab", -1)

    first = passed_along(free_green[0], "slab", -1)
    beyond = lax.fori_loop(0, lax.axis_size("slab") - 2, advance, first)
    green = sweep(beyond)
    self_energy = self_energy_of(green[0, 0], occupation, phonon_weight, phonon_mode)
    return green[None], self_energy.reshape(green.shape)[None]


def solution(mesh):
    in_specs = (
        P("slab", "energy", "kmom", None, None, None),
        P("slab", None, None),
        P("slab", None, None),
        P("energy"),
        P(),
        P(),
    )
    out_specs = (
        P("slab", "energy", "kmom", None, None, None),
        P("slab", "energy", "kmom", None, None, None),
    )
    return jax.shard_map(
        on_device, mesh=mesh, in_specs=in_specs, out_specs=out_specs, check_vma=False
    )
```

```python
import jax
import jax.numpy as jnp
from jax import lax
from jax.sharding import PartitionSpec as P


def passed_along(shard, axis, by):
    length = lax.axis_size(axis)
    pairs = [(i, i + by) for i in range(length) if 0 <= i + by < length]
    return lax.ppermute(shard, axis, pairs)


def complex_product(left_factor, right_factor):
    left_real = left_factor[..., 0, :, :]
    left_imag = left_factor[..., 1, :, :]
    right_real = right_factor[..., 0, :, :]
    right_imag = right_factor[..., 1, :, :]
    high = lax.Precision.HIGH
    real_part = jnp.matmul(left_real, right_real, precision=high) - jnp.matmul(
        left_imag, right_imag, precision=high
    )
    imag_part = jnp.matmul(left_real, right_imag, precision=high) + jnp.matmul(
        left_imag, right_real, precision=high
    )
    return jnp.stack([real_part, imag_part], axis=-3)


def sandwich(pair_map, inner):
    return complex_product(complex_product(pair_map, inner), jnp.swapaxes(pair_map, -1, -2))


def self_energy_of(green, occupation, phonon_weight, phonon_mode):
    filling = occupation[0]
    width = green.shape[-1]
    row = lax.broadcasted_iota(jnp.int32, (width, width), 0)
    col = lax.broadcasted_iota(jnp.int32, (width, width), 1)
    above_diagonal = col > row
    packed = jnp.where(
        above_diagonal,
        -filling * (green[0] - green[0].T),
        -filling * (green[1] + green[1].T),
    ).astype(jnp.bfloat16)
    moms = lax.axis_size("kmom")
    rows = width // moms
    held = lax.all_to_all(packed.reshape(moms, rows, width), "kmom", 0, 0)
    count = lax.axis_size("energy")
    within = [(i, i ^ 1) for i in range(count) if (i ^ 1) < count]
    across = [(i, i + 1 if i % 2 else i - 1) for i in range(count)]
    across = [(i, j) for i, j in across if 0 <= j < count]
    facing = lax.ppermute(held, "energy", across)
    beside = lax.ppermute(held, "energy", within)
    flat = held.reshape(moms, -1).astype(jnp.float32)
    near = beside.reshape(moms, -1).astype(jnp.float32) + facing.reshape(moms, -1).astype(jnp.float32)
    still = phonon_mode[0] == 0
    weight_still = jnp.where(still, phonon_weight[0], phonon_weight[1])
    weight_moved = jnp.where(still, phonon_weight[1], phonon_weight[0])
    summed = jnp.matmul(
        weight_still, flat + flat, precision=lax.Precision.HIGHEST
    ) + jnp.matmul(weight_moved, near, precision=lax.Precision.HIGHEST)
    out = summed.astype(jnp.bfloat16).reshape(moms, rows, width)
    back = lax.all_to_all(out, "kmom", 0, 0).reshape(width, width)
    mirrored = back.T
    real_part = jnp.where(above_diagonal, back, jnp.where(col < row, -mirrored, jnp.zeros_like(back)))
    imag_part = jnp.where(above_diagonal, mirrored, back)
    return jnp.stack([real_part, imag_part], axis=0)


def on_device(free_green, coupling, coupling_tiles, occupation, phonon_weight, phonon_mode):
    slab_count = free_green.shape[0]
    block_width = coupling.shape[-1]
    tile_count = coupling_tiles.shape[1]
    tile_size = block_width // tile_count
    column_tile = jnp.arange(block_width, dtype=jnp.int32) // tile_size
    tile_hit = jnp.any(coupling_tiles[..., None] == column_tile, axis=-2).astype(jnp.float32)
    tile_mask = jnp.broadcast_to(
        tile_hit[:, :, None, :], (slab_count, tile_count, tile_size, block_width)
    ).reshape(slab_count, block_width, block_width)
    coupled = coupling * tile_mask
    pair_map = jnp.einsum(
        "ekcij,jl->ekcil", free_green[0], coupled[0], precision=lax.Precision.HIGHEST
    )[0, 0]
    map_real, map_imag = pair_map[0], pair_map[1]
    left_block = jnp.concatenate(
        [
            jnp.concatenate([map_real, -map_imag], axis=1),
            jnp.concatenate([map_imag, map_real], axis=1),
        ],
        axis=0,
    )
    right_block = jnp.concatenate([map_real.T, map_imag.T], axis=1)
    left_block, right_block = lax.optimization_barrier((left_block, right_block))
    width = block_width
    high = lax.Precision.HIGH

    def sweep(beyond):
        inner = beyond.reshape(2 * width, width)
        mixed = jnp.matmul(left_block, inner, precision=high)
        outer = jnp.matmul(mixed, right_block, precision=high)
        real_part = outer[:width, :width] - outer[width:, width:]
        imag_part = outer[:width, width:] + outer[width:, :width]
        return free_green[0] + jnp.stack([real_part, imag_part], axis=0)[None, None]

    beyond = passed_along(free_green[0], "slab", -1)
    for _ in range(lax.axis_size("slab") - 2):
        beyond = passed_along(sweep(beyond), "slab", -1)
    green = sweep(beyond)
    self_energy = self_energy_of(green[0, 0], occupation, phonon_weight, phonon_mode)
    return green[None], self_energy.reshape(green.shape)[None]


def solution(mesh):
    in_specs = (
        P("slab", "energy", "kmom", None, None, None),
        P("slab", None, None),
        P("slab", None, None),
        P("energy"),
        P(),
        P(),
    )
    out_specs = (
        P("slab", "energy", "kmom", None, None, None),
        P("slab", "energy", "kmom", None, None, None),
    )
    return jax.shard_map(
        on_device, mesh=mesh, in_specs=in_specs, out_specs=out_specs, check_vma=False
    )
```

```python
import jax
import jax.numpy as jnp
from jax import lax
from jax.sharding import PartitionSpec as P


def passed_along(shard, axis, by):
    length = lax.axis_size(axis)
    pairs = [(i, i + by) for i in range(length) if 0 <= i + by < length]
    return lax.ppermute(shard, axis, pairs)


def complex_product(left_factor, right_factor):
    left_real = left_factor[..., 0, :, :]
    left_imag = left_factor[..., 1, :, :]
    right_real = right_factor[..., 0, :, :]
    right_imag = right_factor[..., 1, :, :]
    high = lax.Precision.HIGH
    real_part = jnp.matmul(left_real, right_real, precision=high) - jnp.matmul(
        left_imag, right_imag, precision=high
    )
    imag_part = jnp.matmul(left_real, right_imag, precision=high) + jnp.matmul(
        left_imag, right_real, precision=high
    )
    return jnp.stack([real_part, imag_part], axis=-3)


def sandwich(pair_map, inner):
    return complex_product(complex_product(pair_map, inner), jnp.swapaxes(pair_map, -1, -2))


def self_energy_of(green, occupation, phonon_weight, phonon_mode):
    filling = occupation[0]
    width = green.shape[-1]
    row = lax.broadcasted_iota(jnp.int32, (width, width), 0)
    col = lax.broadcasted_iota(jnp.int32, (width, width), 1)
    above_diagonal = col > row
    packed = jnp.where(
        above_diagonal,
        -filling * (green[0] - green[0].T),
        -filling * (green[1] + green[1].T),
    ).astype(jnp.bfloat16)
    moms = lax.axis_size("kmom")
    rows = width // moms
    count = lax.axis_size("energy")
    within = [(i, i ^ 1) for i in range(count) if (i ^ 1) < count]
    across = [(i, i + 1 if i % 2 else i - 1) for i in range(count)]
    across = [(i, j) for i, j in across if 0 <= j < count]
    beside = lax.ppermute(packed, "energy", within)
    facing = lax.ppermute(packed, "energy", across)
    three = jnp.stack([packed, beside, facing], axis=0).reshape(3, moms, rows, width)
    held = lax.all_to_all(three.transpose(1, 0, 2, 3), "kmom", 0, 0)
    flat = held[:, 0].reshape(moms, -1).astype(jnp.float32)
    near = held[:, 1].reshape(moms, -1).astype(jnp.float32) + held[:, 2].reshape(
        moms, -1
    ).astype(jnp.float32)
    still = phonon_mode[0] == 0
    weight_still = jnp.where(still, phonon_weight[0], phonon_weight[1])
    weight_moved = jnp.where(still, phonon_weight[1], phonon_weight[0])
    summed = jnp.matmul(
        weight_still, flat + flat, precision=lax.Precision.HIGHEST
    ) + jnp.matmul(weight_moved, near, precision=lax.Precision.HIGHEST)
    out = summed.astype(jnp.bfloat16).reshape(moms, rows, width)
    back = lax.all_to_all(out, "kmom", 0, 0).reshape(width, width)
    mirrored = back.T
    real_part = jnp.where(above_diagonal, back, jnp.where(col < row, -mirrored, jnp.zeros_like(back)))
    imag_part = jnp.where(above_diagonal, mirrored, back)
    return jnp.stack([real_part, imag_part], axis=0)


def on_device(free_green, coupling, coupling_tiles, occupation, phonon_weight, phonon_mode):
    slab_count = free_green.shape[0]
    block_width = coupling.shape[-1]
    tile_count = coupling_tiles.shape[1]
    tile_size = block_width // tile_count
    column_tile = jnp.arange(block_width, dtype=jnp.int32) // tile_size
    tile_hit = jnp.any(coupling_tiles[..., None] == column_tile, axis=-2).astype(jnp.float32)
    tile_mask = jnp.broadcast_to(
        tile_hit[:, :, None, :], (slab_count, tile_count, tile_size, block_width)
    ).reshape(slab_count, block_width, block_width)
    coupled = coupling * tile_mask
    pair_map = jnp.einsum(
        "ekcij,jl->ekcil", free_green[0], coupled[0], precision=lax.Precision.HIGHEST
    )[0, 0]
    map_real, map_imag = pair_map[0], pair_map[1]
    left_block = jnp.concatenate(
        [
            jnp.concatenate([map_real, -map_imag], axis=1),
            jnp.concatenate([map_imag, map_real], axis=1),
        ],
        axis=0,
    )
    right_block = jnp.concatenate([map_real.T, map_imag.T], axis=1)
    left_block, right_block = lax.optimization_barrier((left_block, right_block))
    width = block_width
    high = lax.Precision.HIGH

    def sweep(beyond):
        inner = beyond.reshape(2 * width, width)
        mixed = jnp.matmul(left_block, inner, precision=high)
        outer = jnp.matmul(mixed, right_block, precision=high)
        real_part = outer[:width, :width] - outer[width:, width:]
        imag_part = outer[:width, width:] + outer[width:, :width]
        return free_green[0] + jnp.stack([real_part, imag_part], axis=0)[None, None]

    def advance(turn_index, beyond):
        return passed_along(sweep(beyond), "slab", -1)

    first = passed_along(free_green[0], "slab", -1)
    beyond = lax.fori_loop(0, lax.axis_size("slab") - 2, advance, first)
    green = sweep(beyond)
    self_energy = self_energy_of(green[0, 0], occupation, phonon_weight, phonon_mode)
    return green[None], self_energy.reshape(green.shape)[None]


def solution(mesh):
    in_specs = (
        P("slab", "energy", "kmom", None, None, None),
        P("slab", None, None),
        P("slab", None, None),
        P("energy"),
        P(),
        P(),
    )
    out_specs = (
        P("slab", "energy", "kmom", None, None, None),
        P("slab", "energy", "kmom", None, None, None),
    )
    return jax.shard_map(
        on_device, mesh=mesh, in_specs=in_specs, out_specs=out_specs, check_vma=False
    )
```

```python
import jax
import jax.numpy as jnp
from jax import lax
from jax.sharding import PartitionSpec as P


def passed_along(shard, axis, by):
    length = lax.axis_size(axis)
    pairs = [(i, i + by) for i in range(length) if 0 <= i + by < length]
    return lax.ppermute(shard, axis, pairs)


def complex_product(left_factor, right_factor):
    left_real = left_factor[..., 0, :, :]
    left_imag = left_factor[..., 1, :, :]
    right_real = right_factor[..., 0, :, :]
    right_imag = right_factor[..., 1, :, :]
    high = lax.Precision.HIGH
    real_part = jnp.matmul(left_real, right_real, precision=high) - jnp.matmul(
        left_imag, right_imag, precision=high
    )
    imag_part = jnp.matmul(left_real, right_imag, precision=high) + jnp.matmul(
        left_imag, right_real, precision=high
    )
    return jnp.stack([real_part, imag_part], axis=-3)


def sandwich(pair_map, inner):
    return complex_product(complex_product(pair_map, inner), jnp.swapaxes(pair_map, -1, -2))


def self_energy_of(green, occupation, phonon_weight, phonon_mode):
    filling = occupation[0]
    width = green.shape[-1]
    row = lax.broadcasted_iota(jnp.int32, (width, width), 0)
    col = lax.broadcasted_iota(jnp.int32, (width, width), 1)
    above_diagonal = col > row
    packed = jnp.where(
        above_diagonal,
        -filling * (green[0] - green[0].T),
        -filling * (green[1] + green[1].T),
    ).astype(jnp.bfloat16)
    moms = lax.axis_size("kmom")
    rows = width // moms
    held = lax.all_to_all(packed.reshape(moms, rows, width), "kmom", 0, 0)
    count = lax.axis_size("energy")
    within = [(i, i ^ 1) for i in range(count) if (i ^ 1) < count]
    across = [(i, i + 1 if i % 2 else i - 1) for i in range(count)]
    across = [(i, j) for i, j in across if 0 <= j < count]
    beside = lax.ppermute(held, "energy", within)
    facing = lax.ppermute(held, "energy", across)
    flat = held.reshape(moms, -1).astype(jnp.float32)
    near = beside.reshape(moms, -1).astype(jnp.float32) + facing.reshape(moms, -1).astype(jnp.float32)
    still = phonon_mode[0] == 0
    weight_still = jnp.where(still, phonon_weight[0], phonon_weight[1])
    weight_moved = jnp.where(still, phonon_weight[1], phonon_weight[0])
    summed = jnp.matmul(
        weight_still, flat + flat, precision=lax.Precision.HIGHEST
    ) + jnp.matmul(weight_moved, near, precision=lax.Precision.HIGHEST)
    out = summed.astype(jnp.bfloat16).reshape(moms, rows, width)
    back = lax.all_to_all(out, "kmom", 0, 0).reshape(width, width)
    mirrored = back.T
    real_part = jnp.where(above_diagonal, back, jnp.where(col < row, -mirrored, jnp.zeros_like(back)))
    imag_part = jnp.where(above_diagonal, mirrored, back)
    return jnp.stack([real_part, imag_part], axis=0)


def on_device(free_green, coupling, coupling_tiles, occupation, phonon_weight, phonon_mode):
    slab_count = free_green.shape[0]
    block_width = coupling.shape[-1]
    tile_count = coupling_tiles.shape[1]
    tile_size = block_width // tile_count
    column_tile = jnp.arange(block_width, dtype=jnp.int32) // tile_size
    tile_hit = jnp.any(coupling_tiles[..., None] == column_tile, axis=-2).astype(jnp.float32)
    tile_mask = jnp.broadcast_to(
        tile_hit[:, :, None, :], (slab_count, tile_count, tile_size, block_width)
    ).reshape(slab_count, block_width, block_width)
    coupled = coupling * tile_mask
    pair_map = jnp.einsum(
        "ekcij,jl->ekcil", free_green[0], coupled[0], precision=lax.Precision.HIGHEST
    )[0, 0]
    map_real, map_imag = pair_map[0], pair_map[1]
    left_block = jnp.concatenate(
        [
            jnp.concatenate([map_real, -map_imag], axis=1),
            jnp.concatenate([map_imag, map_real], axis=1),
        ],
        axis=0,
    )
    right_block = jnp.concatenate([map_real.T, map_imag.T], axis=1)
    left_block, right_block = lax.optimization_barrier((left_block, right_block))
    width = block_width
    high = lax.Precision.HIGH

    def sweep(beyond):
        inner = beyond.reshape(2 * width, width)
        mixed = jnp.matmul(left_block, inner, precision=high)
        outer = jnp.matmul(mixed, right_block, precision=high)
        real_part = outer[:width, :width] - outer[width:, width:]
        imag_part = outer[:width, width:] + outer[width:, :width]
        return free_green[0] + jnp.stack([real_part, imag_part], axis=0)[None, None]

    def advance(turn_index, beyond):
        return passed_along(sweep(beyond), "slab", -1)

    def held_back(block):
        def spin(turn, acc):
            return jnp.matmul(acc, acc, precision=high)

        seed = lax.optimization_barrier(jnp.full((width, width), 1.0 / width, jnp.float32))
        spun = lax.fori_loop(0, 14, spin, seed)
        return block + spun[0, 0] * 0.0

    late = lax.axis_index("energy") % 2 == 1
    start_block = lax.cond(late, held_back, lambda block: block, free_green[0])
    first = passed_along(start_block, "slab", -1)
    beyond = lax.fori_loop(0, lax.axis_size("slab") - 2, advance, first)
    green = sweep(beyond)
    self_energy = self_energy_of(green[0, 0], occupation, phonon_weight, phonon_mode)
    return green[None], self_energy.reshape(green.shape)[None]


def solution(mesh):
    in_specs = (
        P("slab", "energy", "kmom", None, None, None),
        P("slab", None, None),
        P("slab", None, None),
        P("energy"),
        P(),
        P(),
    )
    out_specs = (
        P("slab", "energy", "kmom", None, None, None),
        P("slab", "energy", "kmom", None, None, None),
    )
    return jax.shard_map(
        on_device, mesh=mesh, in_specs=in_specs, out_specs=out_specs, check_vma=False
    )
```

```python
import jax
import jax.numpy as jnp
from jax import lax
from jax.sharding import PartitionSpec as P


def passed_along(shard, axis, by):
    length = lax.axis_size(axis)
    pairs = [(i, i + by) for i in range(length) if 0 <= i + by < length]
    return lax.ppermute(shard, axis, pairs)


def complex_product(left_factor, right_factor):
    left_real = left_factor[..., 0, :, :]
    left_imag = left_factor[..., 1, :, :]
    right_real = right_factor[..., 0, :, :]
    right_imag = right_factor[..., 1, :, :]
    high = lax.Precision.HIGH
    real_part = jnp.matmul(left_real, right_real, precision=high) - jnp.matmul(
        left_imag, right_imag, precision=high
    )
    imag_part = jnp.matmul(left_real, right_imag, precision=high) + jnp.matmul(
        left_imag, right_real, precision=high
    )
    return jnp.stack([real_part, imag_part], axis=-3)


def sandwich(pair_map, inner):
    return complex_product(complex_product(pair_map, inner), jnp.swapaxes(pair_map, -1, -2))


def self_energy_of(green, occupation, phonon_weight, phonon_mode):
    filling = occupation[0]
    width = green.shape[-1]
    row = lax.broadcasted_iota(jnp.int32, (width, width), 0)
    col = lax.broadcasted_iota(jnp.int32, (width, width), 1)
    above_diagonal = col > row
    packed = jnp.where(
        above_diagonal,
        -filling * (green[0] - green[0].T),
        -filling * (green[1] + green[1].T),
    ).astype(jnp.bfloat16)
    moms = lax.axis_size("kmom")
    rows = width // moms
    held = lax.all_to_all(packed.reshape(moms, rows, width), "kmom", 0, 0)
    count = lax.axis_size("energy")
    within = [(i, i ^ 1) for i in range(count) if (i ^ 1) < count]
    across = [(i, i + 1 if i % 2 else i - 1) for i in range(count)]
    across = [(i, j) for i, j in across if 0 <= j < count]
    beside = lax.ppermute(held, "energy", within)
    facing = lax.ppermute(held, "energy", across)
    flat = held.reshape(moms, -1).astype(jnp.float32)
    near = beside.reshape(moms, -1).astype(jnp.float32) + facing.reshape(moms, -1).astype(jnp.float32)
    still = phonon_mode[0] == 0
    weight_still = jnp.where(still, phonon_weight[0], phonon_weight[1])
    weight_moved = jnp.where(still, phonon_weight[1], phonon_weight[0])
    summed = jnp.matmul(
        weight_still, flat + flat, precision=lax.Precision.HIGHEST
    ) + jnp.matmul(weight_moved, near, precision=lax.Precision.HIGHEST)
    out = summed.astype(jnp.bfloat16).reshape(moms, rows, width)
    back = lax.all_to_all(out, "kmom", 0, 0).reshape(width, width)
    mirrored = back.T
    real_part = jnp.where(above_diagonal, back, jnp.where(col < row, -mirrored, jnp.zeros_like(back)))
    imag_part = jnp.where(above_diagonal, mirrored, back)
    return jnp.stack([real_part, imag_part], axis=0)


def on_device(free_green, coupling, coupling_tiles, occupation, phonon_weight, phonon_mode):
    slab_count = free_green.shape[0]
    block_width = coupling.shape[-1]
    tile_count = coupling_tiles.shape[1]
    tile_size = block_width // tile_count
    column_tile = jnp.arange(block_width, dtype=jnp.int32) // tile_size
    tile_hit = jnp.any(coupling_tiles[..., None] == column_tile, axis=-2).astype(jnp.float32)
    tile_mask = jnp.broadcast_to(
        tile_hit[:, :, None, :], (slab_count, tile_count, tile_size, block_width)
    ).reshape(slab_count, block_width, block_width)
    coupled = coupling * tile_mask
    pair_map = jnp.einsum(
        "ekcij,jl->ekcil", free_green[0], coupled[0], precision=lax.Precision.HIGHEST
    )[0, 0]
    map_real, map_imag = pair_map[0], pair_map[1]
    left_block = jnp.concatenate(
        [
            jnp.concatenate([map_real, -map_imag], axis=1),
            jnp.concatenate([map_imag, map_real], axis=1),
        ],
        axis=0,
    )
    right_block = jnp.concatenate([map_real.T, map_imag.T], axis=1)
    left_block, right_block = lax.optimization_barrier((left_block, right_block))
    width = block_width
    high = lax.Precision.HIGH

    def sweep(beyond):
        inner = beyond.reshape(2 * width, width)
        mixed = jnp.matmul(left_block, inner, precision=high)
        outer = jnp.matmul(mixed, right_block, precision=high)
        real_part = outer[:width, :width] - outer[width:, width:]
        imag_part = outer[:width, width:] + outer[width:, :width]
        return free_green[0] + jnp.stack([real_part, imag_part], axis=0)[None, None]

    slabs = lax.axis_size("slab")
    slab = lax.axis_index("slab")
    beyond = jnp.zeros(free_green.shape[1:], jnp.float32)
    sent = free_green[0]
    for source in range(slabs - 1, 0, -1):
        if source < slabs - 1:
            sent = sweep(beyond)
        arrived = lax.ppermute(sent, "slab", [(source, source - 1)])
        beyond = jnp.where(slab == source - 1, arrived, beyond)
    green = sweep(beyond)
    self_energy = self_energy_of(green[0, 0], occupation, phonon_weight, phonon_mode)
    return green[None], self_energy.reshape(green.shape)[None]


def solution(mesh):
    in_specs = (
        P("slab", "energy", "kmom", None, None, None),
        P("slab", None, None),
        P("slab", None, None),
        P("energy"),
        P(),
        P(),
    )
    out_specs = (
        P("slab", "energy", "kmom", None, None, None),
        P("slab", "energy", "kmom", None, None, None),
    )
    return jax.shard_map(
        on_device, mesh=mesh, in_specs=in_specs, out_specs=out_specs, check_vma=False
    )
```

```python
import jax
import jax.numpy as jnp
from jax import lax
from jax.sharding import PartitionSpec as P


def passed_along(shard, axis, by):
    length = lax.axis_size(axis)
    pairs = [(i, i + by) for i in range(length) if 0 <= i + by < length]
    return lax.ppermute(shard, axis, pairs)


def complex_product(left_factor, right_factor):
    left_real = left_factor[..., 0, :, :]
    left_imag = left_factor[..., 1, :, :]
    right_real = right_factor[..., 0, :, :]
    right_imag = right_factor[..., 1, :, :]
    high = lax.Precision.HIGH
    real_part = jnp.matmul(left_real, right_real, precision=high) - jnp.matmul(
        left_imag, right_imag, precision=high
    )
    imag_part = jnp.matmul(left_real, right_imag, precision=high) + jnp.matmul(
        left_imag, right_real, precision=high
    )
    return jnp.stack([real_part, imag_part], axis=-3)


def sandwich(pair_map, inner):
    return complex_product(complex_product(pair_map, inner), jnp.swapaxes(pair_map, -1, -2))


def self_energy_of(green, occupation, phonon_weight, phonon_mode):
    filling = occupation[0]
    width = green.shape[-1]
    row = lax.broadcasted_iota(jnp.int32, (width, width), 0)
    col = lax.broadcasted_iota(jnp.int32, (width, width), 1)
    above_diagonal = col > row
    packed = jnp.where(
        above_diagonal,
        -filling * (green[0] - green[0].T),
        -filling * (green[1] + green[1].T),
    ).astype(jnp.bfloat16)
    moms = lax.axis_size("kmom")
    rows = width // moms
    held = lax.all_to_all(packed.reshape(moms, rows, width), "kmom", 0, 0)
    count = lax.axis_size("energy")
    within = [(i, i ^ 1) for i in range(count) if (i ^ 1) < count]
    across = [(i, i + 1 if i % 2 else i - 1) for i in range(count)]
    across = [(i, j) for i, j in across if 0 <= j < count]
    beside = lax.ppermute(held, "energy", within)
    facing = lax.ppermute(held, "energy", across)
    flat = held.reshape(moms, -1).astype(jnp.float32)
    near = beside.reshape(moms, -1).astype(jnp.float32) + facing.reshape(moms, -1).astype(jnp.float32)
    still = phonon_mode[0] == 0
    weight_still = jnp.where(still, phonon_weight[0], phonon_weight[1])
    weight_moved = jnp.where(still, phonon_weight[1], phonon_weight[0])
    summed = jnp.matmul(
        weight_still, flat + flat, precision=lax.Precision.HIGH
    ) + jnp.matmul(weight_moved, near, precision=lax.Precision.HIGH)
    out = summed.astype(jnp.bfloat16).reshape(moms, rows, width)
    back = lax.all_to_all(out, "kmom", 0, 0).reshape(width, width)
    mirrored = back.T
    real_part = jnp.where(above_diagonal, back, jnp.where(col < row, -mirrored, jnp.zeros_like(back)))
    imag_part = jnp.where(above_diagonal, mirrored, back)
    return jnp.stack([real_part, imag_part], axis=0)


def on_device(free_green, coupling, coupling_tiles, occupation, phonon_weight, phonon_mode):
    slab_count = free_green.shape[0]
    block_width = coupling.shape[-1]
    tile_count = coupling_tiles.shape[1]
    tile_size = block_width // tile_count
    column_tile = jnp.arange(block_width, dtype=jnp.int32) // tile_size
    tile_hit = jnp.any(coupling_tiles[..., None] == column_tile, axis=-2).astype(jnp.float32)
    tile_mask = jnp.broadcast_to(
        tile_hit[:, :, None, :], (slab_count, tile_count, tile_size, block_width)
    ).reshape(slab_count, block_width, block_width)
    coupled = coupling * tile_mask
    pair_map = jnp.einsum(
        "ekcij,jl->ekcil", free_green[0], coupled[0], precision=lax.Precision.HIGHEST
    )[0, 0]
    map_real, map_imag = pair_map[0], pair_map[1]
    left_block = jnp.concatenate(
        [
            jnp.concatenate([map_real, -map_imag], axis=1),
            jnp.concatenate([map_imag, map_real], axis=1),
        ],
        axis=0,
    )
    right_block = jnp.concatenate([map_real.T, map_imag.T], axis=1)
    left_block, right_block = lax.optimization_barrier((left_block, right_block))
    width = block_width
    high = lax.Precision.HIGH

    def sweep(beyond):
        inner = beyond.reshape(2 * width, width)
        mixed = jnp.matmul(left_block, inner, precision=high)
        outer = jnp.matmul(mixed, right_block, precision=high)
        real_part = outer[:width, :width] - outer[width:, width:]
        imag_part = outer[:width, width:] + outer[width:, :width]
        return free_green[0] + jnp.stack([real_part, imag_part], axis=0)[None, None]

    def advance(turn_index, beyond):
        return passed_along(sweep(beyond), "slab", -1)

    first = passed_along(free_green[0], "slab", -1)
    beyond = lax.fori_loop(0, lax.axis_size("slab") - 2, advance, first)
    green = sweep(beyond)
    self_energy = self_energy_of(green[0, 0], occupation, phonon_weight, phonon_mode)
    return green[None], self_energy.reshape(green.shape)[None]


def solution(mesh):
    in_specs = (
        P("slab", "energy", "kmom", None, None, None),
        P("slab", None, None),
        P("slab", None, None),
        P("energy"),
        P(),
        P(),
    )
    out_specs = (
        P("slab", "energy", "kmom", None, None, None),
        P("slab", "energy", "kmom", None, None, None),
    )
    return jax.shard_map(
        on_device, mesh=mesh, in_specs=in_specs, out_specs=out_specs, check_vma=False
    )
```
